128 devices in a mesh: own: 32 (over y, z, core), vir: 4 (over x).
Axes of the slice: x: 4, y: 4, z: 4, core: 2. Of those that a mesh axis runs over, the one named last changes fastest.
Arguments:
- amplitudes: float32 [384, 512, 1024], P('vir', 'own'), may hold values from -6 to 6
- pair_live: int32 [384, 512], P('vir', 'own'), may hold values 0 or 1
- ladder_integrals: float32 [1024, 1024], P('own'), may hold values from -0.1875 to 0.1875
- cycle_integrals: float32 [512, 32, 128], P('vir'), may hold values from -0.046875 to 0.046875
Outputs:
- ladder_part: float32 [384, 512, 1024], P('vir', 'own')
- cycle_part: float32 [384, 32, 128], P('vir', 'own')
The draws below stay inside these ranges and needn't reach their ends.
All inputs are finite; a program needn't handle non-finite values. No bound on the sum of `pair_live` on one device may be relied on, other than what follows from the above.
Results may differ from the reference program's by a relative error of at most 0.00007.
Values sent between devices are 32-bit elements; how exact they have to be, the bound alone decides.
No kernel may reach another device: no remote copies, remote signals or barrier semaphores. Data moves between devices by JAX's collectives and lax.ppermute only.
A program may use at most 128 MiB of HBM per device.

```python
import jax
import jax.numpy as jnp
from jax import lax

NV = 32
NRJ = 4
NI = 384
NJ = 512
NV2 = 1024


def touch_ends(array, rng, low, top_value):
    longest = array.shape.index(max(array.shape))
    spots = []
    for shift in (0, 1):
        where = [jax.random.randint(jax.random.fold_in(rng, axis), (), 0, length) for axis, length in enumerate(array.shape)]
        where[longest] = (where[longest] + shift) % array.shape[longest]
        spots.append(tuple(where))
    return array.at[spots[0]].set(low).at[spots[1]].set(top_value)


def block_levels(key, extent, cuts, least, top_value):
    level, own = 1.0, jax.random.fold_in(key, 6)
    for position, parts in cuts:
        heights = jnp.exp(jax.random.uniform(jax.random.fold_in(own, position), (parts,), jnp.float32, least / len(cuts), top_value / len(cuts)))
        level = level * jnp.repeat(heights, extent[position] // parts).reshape([-1 if axis == position else 1 for axis in range(len(extent))])
    return level


def noise(key, shape, scale, most, split=(), held_as=jnp.bfloat16):
    entries = jax.random.normal(key, shape, jnp.float32) * scale
    if len(split) > 0:
        entries = block_levels(key, shape, split, -0.22, 0.18) * entries
    return jnp.clip(entries, min=-most, max=most).astype(held_as)


def setup_inputs(seed: int = 0) -> dict:
    splits = jax.random.split(jax.random.key(seed), 5)
    return {
        "amplitudes": noise(splits[0], (NI, NJ, NV2), 1.0, 6.0, ((0, 4), (1, 32)), jnp.float32),
        "pair_live": touch_ends((jax.random.randint(splits[1], (NI, NJ), 0, 4) < 3).astype(jnp.int32), jax.random.fold_in(splits[1], 1), 0, 1),
        "ladder_integrals": noise(splits[2], (NV2, NV2), NV2 ** -0.5, 0.1875, ((0, 32),), jnp.float32),
        "cycle_integrals": noise(splits[3], (NJ, NV, NRJ * NV), (NJ * NV) ** -0.5, 0.046875, ((0, 4),), jnp.float32),
    }


def reference(amplitudes, pair_live, ladder_integrals, cycle_integrals):
    live = pair_live.astype(jnp.float32)
    screened = amplitudes * live[:, :, None]
    flat = screened.reshape(NI * NJ, NV2)
    ladder = jnp.dot(flat, ladder_integrals, precision=lax.Precision.HIGHEST, preferred_element_type=jnp.float32)
    ladder_part = ladder.reshape(NI, NJ, NV2) * live[:, :, None]
    blocks = screened.reshape(NI, NJ, NV, NV).transpose(0, 2, 1, 3).reshape(NI * NV, NJ * NV)
    cycle = jnp.dot(blocks, cycle_integrals.reshape(NJ * NV, NRJ * NV), precision=lax.Precision.HIGHEST, preferred_element_type=jnp.float32)
    cycle_part = cycle.reshape(NI, NV, NRJ * NV)
    return ladder_part, cycle_part
```

```python
import jax
import jax.numpy as jnp
from jax import lax
from jax.sharding import PartitionSpec as P


def cycle_piece(cycle_integrals, kblock):
    own = lax.axis_index("own")
    held = cycle_integrals.shape[0]
    start = own * kblock
    piece = lax.dynamic_slice_in_dim(cycle_integrals, start % held, kblock, axis=0)
    pieces = lax.all_gather(piece, "vir")
    return lax.dynamic_index_in_dim(pieces, start // held, axis=0, keepdims=False)


def local(amplitudes, pair_live, ladder_integrals, cycle_integrals):
    live = pair_live.astype(jnp.float32)
    screened = amplitudes * live[:, :, None]
    first_rows = screened.shape[0]
    second_rows = screened.shape[1]
    width = screened.shape[2]
    virtuals = cycle_integrals.shape[1]

    weights = cycle_piece(cycle_integrals, second_rows)
    split = screened.reshape(first_rows, second_rows, width // virtuals, virtuals)
    partial_value = jnp.einsum(
        "ikac,kcm->iam",
        split,
        weights,
        precision=lax.Precision.HIGHEST,
        preferred_element_type=jnp.float32,
    )
    cycle_part = lax.psum_scatter(partial_value, "own", scatter_dimension=1, tiled=True)

    flat = screened.reshape(first_rows * second_rows, width)
    ladder = jnp.dot(
        flat,
        lax.all_gather(ladder_integrals, "own", axis=0, tiled=True),
        precision=lax.Precision.HIGHEST,
        preferred_element_type=jnp.float32,
    )
    ladder_part = ladder.reshape(first_rows, second_rows, width) * live[:, :, None]
    return (ladder_part, cycle_part)


def solution(mesh):
    placed = (P("vir", "own", None), P("vir", "own"), P("own", None), P("vir", None, None))
    return jax.shard_map(
        local,
        mesh=mesh,
        in_specs=placed,
        out_specs=(P("vir", "own", None), P("vir", "own", None)),
        check_vma=False,
    )
```

```python
import jax
import jax.numpy as jnp
from jax import lax
from jax.sharding import PartitionSpec as P


def cycle_piece(cycle_integrals, kblock):
    own = lax.axis_index("own")
    vir = lax.axis_index("vir")
    n_own = lax.axis_size("own")
    n_vir = lax.axis_size("vir")
    held = cycle_integrals.shape[0]
    start = own * kblock
    piece = lax.dynamic_slice_in_dim(cycle_integrals, start % held, kblock, axis=0)
    holder = start // held
    chosen = piece
    for shift in range(1, n_vir):
        pairs = []
        for o in range(n_own):
            src = (o * kblock) // held
            dst = (src + shift) % n_vir
            pairs.append((o * n_vir + src, o * n_vir + dst))
        got = lax.ppermute(piece, ("own", "vir"), pairs)
        chosen = jnp.where((vir - holder) % n_vir == shift, got, chosen)
    return chosen


def local(amplitudes, pair_live, ladder_integrals, cycle_integrals):
    live = pair_live.astype(jnp.float32)
    screened = amplitudes * live[:, :, None]
    first_rows = screened.shape[0]
    second_rows = screened.shape[1]
    width = screened.shape[2]
    virtuals = cycle_integrals.shape[1]

    weights = cycle_piece(cycle_integrals, second_rows)
    split = screened.reshape(first_rows, second_rows, width // virtuals, virtuals)
    partial_value = jnp.einsum(
        "ikac,kcm->aim",
        split,
        weights,
        precision=lax.Precision.HIGHEST,
        preferred_element_type=jnp.float32,
    )
    gathered = lax.all_to_all(partial_value, "own", split_axis=0, concat_axis=0, tiled=True)
    cycle_part = jnp.sum(gathered, axis=0)[:, None, :]

    flat = screened.reshape(first_rows * second_rows, width)
    ladder = jnp.dot(
        flat,
        lax.all_gather(ladder_integrals, "own", axis=0, tiled=True),
        precision=lax.Precision.HIGHEST,
        preferred_element_type=jnp.float32,
    )
    ladder_part = ladder.reshape(first_rows, second_rows, width) * live[:, :, None]
    return (ladder_part, cycle_part)


def solution(mesh):
    placed = (P("vir", "own", None), P("vir", "own"), P("own", None), P("vir", None, None))
    return jax.shard_map(
        local,
        mesh=mesh,
        in_specs=placed,
        out_specs=(P("vir", "own", None), P("vir", "own", None)),
        check_vma=False,
    )
```

```python
import jax
import jax.numpy as jnp
from jax import lax
from jax.sharding import PartitionSpec as P

CORES = 2


def cycle_piece(cycle_integrals, kblock):
    own = lax.axis_index("own")
    vir = lax.axis_index("vir")
    n_own = lax.axis_size("own")
    n_vir = lax.axis_size("vir")
    held = cycle_integrals.shape[0]
    start = own * kblock
    piece = lax.dynamic_slice_in_dim(cycle_integrals, start % held, kblock, axis=0)
    holder = start // held
    chosen = piece
    for shift in range(1, n_vir):
        pairs = []
        for o in range(n_own):
            src = (o * kblock) // held
            dst = (src + shift) % n_vir
            pairs.append((o * n_vir + src, o * n_vir + dst))
        got = lax.ppermute(piece, ("own", "vir"), pairs)
        chosen = jnp.where((vir - holder) % n_vir == shift, got, chosen)
    return chosen


def core_stage(partial_value):
    own = lax.axis_index("own")
    n_own = lax.axis_size("own")
    core = own % CORES
    rest = partial_value.shape[1:]
    by_core = partial_value.reshape((-1, CORES) + rest)
    mine = lax.dynamic_index_in_dim(by_core, core, axis=1, keepdims=False)
    theirs = lax.dynamic_index_in_dim(by_core, 1 - core, axis=1, keepdims=False)
    return mine + lax.ppermute(theirs, "own", [(o, o ^ 1) for o in range(n_own)])


def chip_sends(chip_blocks):
    own = lax.axis_index("own")
    n_own = lax.axis_size("own")
    chips = n_own // CORES
    chip = own // CORES
    mine = lax.dynamic_index_in_dim(chip_blocks, chip, axis=0, keepdims=False)
    received = [mine]
    for shift in range(1, chips):
        outgoing = lax.dynamic_index_in_dim(chip_blocks, (chip + shift) % chips, axis=0, keepdims=False)
        pairs = [(o, ((o // CORES + shift) % chips) * CORES + o % CORES) for o in range(n_own)]
        received.append(lax.ppermute(outgoing, "own", pairs))
    return received


def local(amplitudes, pair_live, ladder_integrals, cycle_integrals):
    live = pair_live.astype(jnp.float32)
    screened = amplitudes * live[:, :, None]
    first_rows = screened.shape[0]
    second_rows = screened.shape[1]
    width = screened.shape[2]
    virtuals = cycle_integrals.shape[1]

    weights = cycle_piece(cycle_integrals, second_rows)
    split = screened.reshape(first_rows, second_rows, width // virtuals, virtuals)
    partial_value = jnp.einsum(
        "ikac,kcm->aim",
        split,
        weights,
        precision=lax.Precision.HIGHEST,
        preferred_element_type=jnp.float32,
    )
    received = chip_sends(core_stage(partial_value))

    flat = screened.reshape(first_rows * second_rows, width)
    ladder = jnp.dot(
        flat,
        lax.all_gather(ladder_integrals, "own", axis=0, tiled=True),
        precision=lax.Precision.HIGH,
        preferred_element_type=jnp.float32,
    )
    ladder_part = ladder.reshape(first_rows, second_rows, width) * live[:, :, None]
    ladder_part, received = lax.optimization_barrier((ladder_part, received))
    cycle_part = sum(received[1:], received[0])[:, None, :]
    return (ladder_part, cycle_part)


def solution(mesh):
    placed = (P("vir", "own", None), P("vir", "own"), P("own", None), P("vir", None, None))
    return jax.shard_map(
        local,
        mesh=mesh,
        in_specs=placed,
        out_specs=(P("vir", "own", None), P("vir", "own", None)),
        check_vma=False,
    )
```

```python
import jax
import jax.numpy as jnp
from jax import lax
from jax.sharding import PartitionSpec as P

def cycle_piece(cycle_integrals, kblock):
    own = lax.axis_index("own")
    vir = lax.axis_index("vir")
    n_own = lax.axis_size("own")
    n_vir = lax.axis_size("vir")
    held = cycle_integrals.shape[0]
    start = own * kblock
    piece = lax.dynamic_slice_in_dim(cycle_integrals, start % held, kblock, axis=0)
    holder = start // held
    chosen = piece
    for shift in range(1, n_vir):
        pairs = []
        for o in range(n_own):
            src = (o * kblock) // held
            dst = (src + shift) % n_vir
            pairs.append((o * n_vir + src, o * n_vir + dst))
        got = lax.ppermute(piece, ("own", "vir"), pairs)
        chosen = jnp.where((vir - holder) % n_vir == shift, got, chosen)
    return chosen


def local(amplitudes, pair_live, ladder_integrals, cycle_integrals):
    live = pair_live.astype(jnp.float32)
    screened = amplitudes * live[:, :, None]
    first_rows = screened.shape[0]
    second_rows = screened.shape[1]
    width = screened.shape[2]
    virtuals = cycle_integrals.shape[1]

    weights = cycle_piece(cycle_integrals, second_rows)
    split = screened.reshape(first_rows, second_rows, width // virtuals, virtuals)
    partial_value = jnp.einsum(
        "ikac,kcm->aim",
        split,
        weights,
        precision=lax.Precision.HIGH,
        preferred_element_type=jnp.float32,
    )
    gathered = lax.all_to_all(partial_value, "own", split_axis=0, concat_axis=0, tiled=True)
    cycle_part = jnp.sum(gathered, axis=0)[:, None, :]

    flat = screened.reshape(first_rows * second_rows, width)
    ladder = jnp.dot(
        flat,
        lax.all_gather(ladder_integrals, "own", axis=0, tiled=True),
        precision=lax.Precision.HIGH,
        preferred_element_type=jnp.float32,
    )
    ladder_part = ladder.reshape(first_rows, second_rows, width) * live[:, :, None]
    return (ladder_part, cycle_part)


def solution(mesh):
    placed = (P("vir", "own", None), P("vir", "own"), P("own", None), P("vir", None, None))
    return jax.shard_map(
        local,
        mesh=mesh,
        in_specs=placed,
        out_specs=(P("vir", "own", None), P("vir", "own", None)),
        check_vma=False,
    )
```

```python
import jax
import jax.numpy as jnp
from jax import lax
from jax.sharding import Mesh
from jax.sharding import PartitionSpec as P

PARTS = ("y", "z", "core")
CHIPS = ("y", "z")


def cycle_piece(cycle_integrals, kblock):
    own = lax.axis_index(PARTS)
    vir = lax.axis_index("vir")
    n_own = lax.axis_size(PARTS)
    n_vir = lax.axis_size("vir")
    held = cycle_integrals.shape[0]
    start = own * kblock
    piece = lax.dynamic_slice_in_dim(cycle_integrals, start % held, kblock, axis=0)
    holder = start // held
    chosen = piece
    for shift in range(1, n_vir):
        pairs = []
        for o in range(n_own):
            src = (o * kblock) // held
            dst = (src + shift) % n_vir
            pairs.append((o * n_vir + src, o * n_vir + dst))
        got = lax.ppermute(piece, PARTS + ("vir",), pairs)
        chosen = jnp.where((vir - holder) % n_vir == shift, got, chosen)
    return chosen


def cycle_reduce(partial_value):
    cores = lax.axis_size("core")
    core = lax.axis_index("core")
    rest = partial_value.shape[1:]
    by_core = partial_value.reshape((-1, cores) + rest)
    mine = lax.dynamic_index_in_dim(by_core, core, axis=1, keepdims=False)
    theirs = lax.dynamic_index_in_dim(by_core, (core + 1) % cores, axis=1, keepdims=False)
    pairs = [(c, (c + 1) % cores) for c in range(cores)]
    chip_share = mine + lax.ppermute(theirs, "core", pairs)
    gathered = lax.all_to_all(chip_share, CHIPS, split_axis=0, concat_axis=0, tiled=True)
    return jnp.sum(gathered, axis=0)[:, None, :]


def local(amplitudes, pair_live, ladder_integrals, cycle_integrals):
    live = pair_live.astype(jnp.float32)
    screened = amplitudes * live[:, :, None]
    first_rows = screened.shape[0]
    second_rows = screened.shape[1]
    width = screened.shape[2]
    virtuals = cycle_integrals.shape[1]

    weights = cycle_piece(cycle_integrals, second_rows)
    split = screened.reshape(first_rows, second_rows, width // virtuals, virtuals)
    partial_value = jnp.einsum(
        "ikac,kcm->aim",
        split,
        weights,
        precision=lax.Precision.HIGH,
        preferred_element_type=jnp.float32,
    )
    cycle_part = cycle_reduce(partial_value)

    flat = screened.reshape(first_rows * second_rows, width)
    ladder = jnp.dot(
        flat,
        lax.all_gather(ladder_integrals, PARTS, axis=0, tiled=True),
        precision=lax.Precision.HIGH,
        preferred_element_type=jnp.float32,
    )
    ladder_part = ladder.reshape(first_rows, second_rows, width) * live[:, :, None]
    return (ladder_part, cycle_part)


def solution(mesh):
    sizes = (4, 4, 2)
    named = Mesh(mesh.devices.reshape(sizes + (mesh.shape["vir"],)), PARTS + ("vir",))
    assert mesh.axis_names == ("own", "vir") and mesh.shape["own"] == 32
    placed = (P("vir", PARTS, None), P("vir", PARTS), P(PARTS, None), P("vir", None, None))
    return jax.shard_map(
        local,
        mesh=named,
        in_specs=placed,
        out_specs=(P("vir", PARTS, None), P("vir", PARTS, None)),
        check_vma=False,
    )
```

```python
import jax
import jax.numpy as jnp
from jax import lax
from jax.experimental import pallas as pl
from jax.experimental.pallas import tpu as pltpu
from jax.sharding import Mesh
from jax.sharding import PartitionSpec as P

PARTS = ("y", "z", "core")
CHIPS = ("y", "z")


def cycle_piece(cycle_integrals, kblock):
    own = lax.axis_index(PARTS)
    vir = lax.axis_index("vir")
    n_own = lax.axis_size(PARTS)
    n_vir = lax.axis_size("vir")
    held = cycle_integrals.shape[0]
    start = own * kblock
    piece = lax.dynamic_slice_in_dim(cycle_integrals, start % held, kblock, axis=0)
    holder = start // held
    chosen = piece
    for shift in range(1, n_vir):
        pairs = []
        for o in range(n_own):
            src = (o * kblock) // held
            dst = (src + shift) % n_vir
            pairs.append((o * n_vir + src, o * n_vir + dst))
        got = lax.ppermute(piece, PARTS + ("vir",), pairs)
        chosen = jnp.where((vir - holder) % n_vir == shift, got, chosen)
    return chosen


def cycle_reduce(partial_value):
    cores = lax.axis_size("core")
    core = lax.axis_index("core")
    rest = partial_value.shape[1:]
    by_core = partial_value.reshape((-1, cores) + rest)
    mine = lax.dynamic_index_in_dim(by_core, core, axis=1, keepdims=False)
    theirs = lax.dynamic_index_in_dim(by_core, (core + 1) % cores, axis=1, keepdims=False)
    pairs = [(c, (c + 1) % cores) for c in range(cores)]
    chip_share = mine + lax.ppermute(theirs, "core", pairs)
    gathered = lax.all_to_all(chip_share, CHIPS, split_axis=0, concat_axis=0, tiled=True)
    return jnp.sum(gathered, axis=0)[:, None, :]


def screen_kernel(live_ref, amp_ref, out_ref):
    n_a, _, rows = out_ref.shape
    nc = amp_ref.shape[2] // n_a
    for k in range(amp_ref.shape[1]):
        flipped = (amp_ref[:, k, :] * live_ref[:, k:k + 1]).T
        out_ref[:, k * nc:(k + 1) * nc, :] = flipped.reshape(n_a, nc, rows)


def screened_by_a(amplitudes, live, virtuals):
    rows, kblock, width = amplitudes.shape
    return pl.pallas_call(
        screen_kernel,
        out_shape=jax.ShapeDtypeStruct((width // virtuals, kblock * virtuals, rows), jnp.float32),
        in_specs=[pl.BlockSpec(memory_space=pltpu.VMEM), pl.BlockSpec(memory_space=pltpu.VMEM)],
        out_specs=pl.BlockSpec(memory_space=pltpu.VMEM),
    )(live, amplitudes)


def local(amplitudes, pair_live, ladder_integrals, cycle_integrals):
    live = pair_live.astype(jnp.float32)
    screened = amplitudes * live[:, :, None]
    first_rows = screened.shape[0]
    second_rows = screened.shape[1]
    width = screened.shape[2]
    virtuals = cycle_integrals.shape[1]

    weights = cycle_piece(cycle_integrals, second_rows)
    split = screened_by_a(amplitudes, live, virtuals).reshape(width // virtuals, second_rows, virtuals, first_rows)
    partial_value = jnp.einsum(
        "akci,kcm->aim",
        split,
        weights,
        precision=lax.Precision.HIGH,
        preferred_element_type=jnp.float32,
    )
    cycle_part = cycle_reduce(partial_value)

    flat = screened.reshape(first_rows * second_rows, width)
    ladder = jnp.dot(
        flat,
        lax.all_gather(ladder_integrals, PARTS, axis=0, tiled=True),
        precision=lax.Precision.HIGH,
        preferred_element_type=jnp.float32,
    )
    ladder_part = ladder.reshape(first_rows, second_rows, width) * live[:, :, None]
    return (ladder_part, cycle_part)


def solution(mesh):
    sizes = (4, 4, 2)
    named = Mesh(mesh.devices.reshape(sizes + (mesh.shape["vir"],)), PARTS + ("vir",))
    assert mesh.axis_names == ("own", "vir") and mesh.shape["own"] == 32
    placed = (P("vir", PARTS, None), P("vir", PARTS), P(PARTS, None), P("vir", None, None))
    return jax.shard_map(
        local,
        mesh=named,
        in_specs=placed,
        out_specs=(P("vir", PARTS, None), P("vir", PARTS, None)),
        check_vma=False,
    )
```

```python
import jax
import jax.numpy as jnp
from jax import lax
from jax.experimental import pallas as pl
from jax.experimental.pallas import tpu as pltpu
from jax.sharding import Mesh
from jax.sharding import PartitionSpec as P

PARTS = ("y", "z", "core")
CHIPS = ("y", "z")


def cycle_piece(cycle_integrals, kblock):
    own = lax.axis_index(PARTS)
    vir = lax.axis_index("vir")
    n_own = lax.axis_size(PARTS)
    n_vir = lax.axis_size("vir")
    held = cycle_integrals.shape[0]
    start = own * kblock
    piece = lax.dynamic_slice_in_dim(cycle_integrals, start % held, kblock, axis=0)
    holder = start // held
    chosen = piece
    for shift in range(1, n_vir):
        pairs = []
        for o in range(n_own):
            src = (o * kblock) // held
            dst = (src + shift) % n_vir
            pairs.append((o * n_vir + src, o * n_vir + dst))
        got = lax.ppermute(piece, PARTS + ("vir",), pairs)
        chosen = jnp.where((vir - holder) % n_vir == shift, got, chosen)
    return chosen


def cycle_reduce(partial_value):
    cores = lax.axis_size("core")
    core = lax.axis_index("core")
    rest = partial_value.shape[1:]
    by_core = partial_value.reshape((-1, cores) + rest)
    mine = lax.dynamic_index_in_dim(by_core, core, axis=1, keepdims=False)
    theirs = lax.dynamic_index_in_dim(by_core, (core + 1) % cores, axis=1, keepdims=False)
    pairs = [(c, (c + 1) % cores) for c in range(cores)]
    chip_share = mine + lax.ppermute(theirs, "core", pairs)
    gathered = lax.all_to_all(chip_share, CHIPS, split_axis=0, concat_axis=0, tiled=True)
    return jnp.sum(gathered, axis=0)[:, None, :]


def screen_kernel(live_ref, amp_ref, out_ref):
    n_a, _, rows = out_ref.shape
    nc = amp_ref.shape[2] // n_a
    for k in range(amp_ref.shape[1]):
        flipped = (amp_ref[:, k, :] * live_ref[:, k:k + 1]).T
        out_ref[:, k * nc:(k + 1) * nc, :] = flipped.reshape(n_a, nc, rows)


def screened_by_a(amplitudes, live, virtuals):
    rows, kblock, width = amplitudes.shape
    lanes = 128
    per_step = lanes // virtuals
    return pl.pallas_call(
        screen_kernel,
        grid=(width // lanes,),
        out_shape=jax.ShapeDtypeStruct((width // virtuals, kblock * virtuals, rows), jnp.float32),
        in_specs=[
            pl.BlockSpec((rows, kblock), lambda s: (0, 0)),
            pl.BlockSpec((rows, kblock, lanes), lambda s: (0, 0, s)),
        ],
        out_specs=pl.BlockSpec((per_step, kblock * virtuals, rows), lambda s: (s, 0, 0)),
    )(live, amplitudes)


def local(amplitudes, pair_live, ladder_integrals, cycle_integrals):
    live = pair_live.astype(jnp.float32)
    screened = amplitudes * live[:, :, None]
    first_rows = screened.shape[0]
    second_rows = screened.shape[1]
    width = screened.shape[2]
    virtuals = cycle_integrals.shape[1]

    weights = cycle_piece(cycle_integrals, second_rows)
    split = screened_by_a(amplitudes, live, virtuals).reshape(width // virtuals, second_rows, virtuals, first_rows)
    partial_value = jnp.einsum(
        "akci,kcm->aim",
        split,
        weights,
        precision=lax.Precision.HIGH,
        preferred_element_type=jnp.float32,
    )
    cycle_part = cycle_reduce(partial_value)

    flat = screened.reshape(first_rows * second_rows, width)
    ladder = jnp.dot(
        flat,
        lax.all_gather(ladder_integrals, PARTS, axis=0, tiled=True),
        precision=lax.Precision.HIGH,
        preferred_element_type=jnp.float32,
    )
    ladder_part = ladder.reshape(first_rows, second_rows, width) * live[:, :, None]
    return (ladder_part, cycle_part)


def solution(mesh):
    sizes = (4, 4, 2)
    named = Mesh(mesh.devices.reshape(sizes + (mesh.shape["vir"],)), PARTS + ("vir",))
    assert mesh.axis_names == ("own", "vir") and mesh.shape["own"] == 32
    placed = (P("vir", PARTS, None), P("vir", PARTS), P(PARTS, None), P("vir", None, None))
    return jax.shard_map(
        local,
        mesh=named,
        in_specs=placed,
        out_specs=(P("vir", PARTS, None), P("vir", PARTS, None)),
        check_vma=False,
    )
```

```python
import jax
import jax.numpy as jnp
from jax import lax
from jax.experimental import pallas as pl
from jax.experimental.pallas import tpu as pltpu
from jax.sharding import Mesh
from jax.sharding import PartitionSpec as P

PARTS = ("y", "z", "core")


def cycle_piece(cycle_integrals, kblock):
    own = lax.axis_index(PARTS)
    vir = lax.axis_index("vir")
    n_own = lax.axis_size(PARTS)
    n_vir = lax.axis_size("vir")
    held = cycle_integrals.shape[0]
    start = own * kblock
    piece = lax.dynamic_slice_in_dim(cycle_integrals, start % held, kblock, axis=0)
    holder = start // held
    chosen = piece
    for shift in range(1, n_vir):
        pairs = []
        for o in range(n_own):
            src = (o * kblock) // held
            dst = (src + shift) % n_vir
            pairs.append((o * n_vir + src, o * n_vir + dst))
        got = lax.ppermute(piece, PARTS + ("vir",), pairs)
        chosen = jnp.where((vir - holder) % n_vir == shift, got, chosen)
    return chosen


def cycle_reduce(partial_value):
    cores = lax.axis_size("core")
    core = lax.axis_index("core")
    rest = partial_value.shape[1:]
    by_core = partial_value.reshape((-1, cores) + rest)
    mine = lax.dynamic_index_in_dim(by_core, core, axis=1, keepdims=False)
    theirs = lax.dynamic_index_in_dim(by_core, (core + 1) % cores, axis=1, keepdims=False)
    pairs = [(c, (c + 1) % cores) for c in range(cores)]
    chip_share = mine + lax.ppermute(theirs, "core", pairs)
    n_y = lax.axis_size("y")
    by_y = chip_share.reshape((n_y, -1) + rest)
    rows_y = jnp.sum(lax.all_to_all(by_y, "y", split_axis=0, concat_axis=0, tiled=False), axis=0)
    return lax.all_to_all(rows_y, "z", split_axis=0, concat_axis=0, tiled=False)


def screen_kernel(live_ref, amp_ref, out_ref):
    n_a, _, rows = out_ref.shape
    nc = amp_ref.shape[2] // n_a
    for k in range(amp_ref.shape[1]):
        flipped = (amp_ref[:, k, :] * live_ref[:, k:k + 1].astype(jnp.float32)).T
        out_ref[:, k * nc:(k + 1) * nc, :] = flipped.reshape(n_a, nc, rows)


def screened_by_a(amplitudes, live, virtuals):
    rows, kblock, width = amplitudes.shape
    lanes = 128
    per_step = lanes // virtuals
    return pl.pallas_call(
        screen_kernel,
        grid=(width // lanes,),
        out_shape=jax.ShapeDtypeStruct((width // virtuals, kblock * virtuals, rows), jnp.float32),
        in_specs=[
            pl.BlockSpec((rows, kblock), lambda s: (0, 0)),
            pl.BlockSpec((rows, kblock, lanes), lambda s: (0, 0, s)),
        ],
        out_specs=pl.BlockSpec((per_step, kblock * virtuals, rows), lambda s: (s, 0, 0)),
    )(live, amplitudes)


def local(amplitudes, pair_live, ladder_integrals, cycle_integrals):
    live = pair_live.astype(jnp.float32)
    screened = amplitudes * live[:, :, None]
    first_rows = screened.shape[0]
    second_rows = screened.shape[1]
    width = screened.shape[2]
    virtuals = cycle_integrals.shape[1]

    weights = cycle_piece(cycle_integrals, second_rows)
    split = screened_by_a(amplitudes, pair_live, virtuals).reshape(width // virtuals, second_rows, virtuals, first_rows)
    partial_value = jnp.einsum(
        "akci,kcm->aim",
        split,
        weights,
        precision=lax.Precision.HIGH,
        preferred_element_type=jnp.float32,
    )
    cycle_part = cycle_reduce(partial_value)

    flat = screened.reshape(first_rows * second_rows, width)
    ladder = jnp.dot(
        flat,
        lax.all_gather(ladder_integrals, PARTS, axis=0, tiled=True),
        precision=lax.Precision.HIGH,
        preferred_element_type=jnp.float32,
    )
    ladder_part = ladder.reshape(first_rows, second_rows, width) * live[:, :, None]
    ladder_part, cycle_part = lax.optimization_barrier((ladder_part, cycle_part))
    return (ladder_part, jnp.sum(cycle_part, axis=0)[:, None, :])


def solution(mesh):
    sizes = (4, 4, 2)
    named = Mesh(mesh.devices.reshape(sizes + (mesh.shape["vir"],)), PARTS + ("vir",))
    assert mesh.axis_names == ("own", "vir") and mesh.shape["own"] == 32
    placed = (P("vir", PARTS, None), P("vir", PARTS), P(PARTS, None), P("vir", None, None))
    return jax.shard_map(
        local,
        mesh=named,
        in_specs=placed,
        out_specs=(P("vir", PARTS, None), P("vir", PARTS, None)),
        check_vma=False,
    )
```

```python
import jax
import jax.numpy as jnp
from jax import lax
from jax.experimental import pallas as pl
from jax.experimental.pallas import tpu as pltpu
from jax.sharding import Mesh
from jax.sharding import PartitionSpec as P

PARTS = ("y", "z", "core")
CHIPS = ("y", "z")


def cycle_piece(cycle_integrals, kblock):
    own = lax.axis_index(PARTS)
    vir = lax.axis_index("vir")
    n_own = lax.axis_size(PARTS)
    n_vir = lax.axis_size("vir")
    held = cycle_integrals.shape[0]
    start = own * kblock
    piece = lax.dynamic_slice_in_dim(cycle_integrals, start % held, kblock, axis=0)
    holder = start // held
    chosen = piece
    for shift in range(1, n_vir):
        pairs = []
        for o in range(n_own):
            src = (o * kblock) // held
            dst = (src + shift) % n_vir
            pairs.append((o * n_vir + src, o * n_vir + dst))
        got = lax.ppermute(piece, PARTS + ("vir",), pairs)
        chosen = jnp.where((vir - holder) % n_vir == shift, got, chosen)
    return chosen


def cycle_reduce(partial_value):
    cores = lax.axis_size("core")
    core = lax.axis_index("core")
    rest = partial_value.shape[1:]
    by_core = partial_value.reshape((-1, cores) + rest)
    mine = lax.dynamic_index_in_dim(by_core, core, axis=1, keepdims=False)
    theirs = lax.dynamic_index_in_dim(by_core, (core + 1) % cores, axis=1, keepdims=False)
    pairs = [(c, (c + 1) % cores) for c in range(cores)]
    chip_share = mine + lax.ppermute(theirs, "core", pairs)
    return lax.all_to_all(chip_share, CHIPS, split_axis=0, concat_axis=0, tiled=True)


def screen_kernel(live_ref, amp_ref, out_ref):
    n_a, _, rows = out_ref.shape
    nc = amp_ref.shape[2] // n_a
    for k in range(amp_ref.shape[1]):
        flipped = (amp_ref[:, k, :] * live_ref[:, k:k + 1]).T
        out_ref[:, k * nc:(k + 1) * nc, :] = flipped.reshape(n_a, nc, rows)


def screened_by_a(amplitudes, live, virtuals):
    rows, kblock, width = amplitudes.shape
    lanes = 128
    per_step = lanes // virtuals
    return pl.pallas_call(
        screen_kernel,
        grid=(width // lanes,),
        out_shape=jax.ShapeDtypeStruct((width // virtuals, kblock * virtuals, rows), jnp.float32),
        in_specs=[
            pl.BlockSpec((rows, kblock), lambda s: (0, 0)),
            pl.BlockSpec((rows, kblock, lanes), lambda s: (0, 0, s)),
        ],
        out_specs=pl.BlockSpec((per_step, kblock * virtuals, rows), lambda s: (s, 0, 0)),
    )(live, amplitudes)


def local(amplitudes, pair_live, ladder_integrals, cycle_integrals):
    live = pair_live.astype(jnp.float32)
    screened = amplitudes * live[:, :, None]
    first_rows = screened.shape[0]
    second_rows = screened.shape[1]
    width = screened.shape[2]
    virtuals = cycle_integrals.shape[1]

    weights = cycle_piece(cycle_integrals, second_rows)
    split = screened_by_a(amplitudes, live, virtuals).reshape(width // virtuals, second_rows, virtuals, first_rows)
    partial_value = jnp.einsum(
        "akci,kcm->aim",
        split,
        weights,
        precision=lax.Precision.HIGH,
        preferred_element_type=jnp.float32,
    )
    cycle_part = cycle_reduce(partial_value)

    flat = screened.reshape(first_rows * second_rows, width)
    ladder = jnp.dot(
        flat,
        lax.all_gather(ladder_integrals, PARTS, axis=0, tiled=True),
        precision=lax.Precision.HIGH,
        preferred_element_type=jnp.float32,
    )
    ladder_part = ladder.reshape(first_rows, second_rows, width) * live[:, :, None]
    ladder_part, cycle_part = lax.optimization_barrier((ladder_part, cycle_part))
    return (ladder_part, jnp.sum(cycle_part, axis=0)[:, None, :])


def solution(mesh):
    sizes = (4, 4, 2)
    named = Mesh(mesh.devices.reshape(sizes + (mesh.shape["vir"],)), PARTS + ("vir",))
    assert mesh.axis_names == ("own", "vir") and mesh.shape["own"] == 32
    placed = (P("vir", PARTS, None), P("vir", PARTS), P(PARTS, None), P("vir", None, None))
    return jax.shard_map(
        local,
        mesh=named,
        in_specs=placed,
        out_specs=(P("vir", PARTS, None), P("vir", PARTS, None)),
        check_vma=False,
    )
```

```python
import jax
import jax.numpy as jnp
from jax import lax
from jax.experimental import pallas as pl
from jax.experimental.pallas import tpu as pltpu
from jax.sharding import Mesh
from jax.sharding import PartitionSpec as P

PARTS = ("y", "z", "core")
CHIPS = ("y", "z")


def cycle_piece(cycle_integrals, kblock):
    own = lax.axis_index(PARTS)
    vir = lax.axis_index("vir")
    n_own = lax.axis_size(PARTS)
    n_vir = lax.axis_size("vir")
    held = cycle_integrals.shape[0]
    start = own * kblock
    piece = lax.dynamic_slice_in_dim(cycle_integrals, start % held, kblock, axis=0)
    holder = start // held
    chosen = piece
    for shift in range(1, n_vir):
        pairs = []
        for o in range(n_own):
            src = (o * kblock) // held
            dst = (src + shift) % n_vir
            pairs.append((o * n_vir + src, o * n_vir + dst))
        got = lax.ppermute(piece, PARTS + ("vir",), pairs)
        chosen = jnp.where((vir - holder) % n_vir == shift, got, chosen)
    return chosen


def cycle_reduce(partial_value):
    cores = lax.axis_size("core")
    core = lax.axis_index("core")
    rest = partial_value.shape[1:]
    by_core = partial_value.reshape((-1, cores) + rest)
    mine = lax.dynamic_index_in_dim(by_core, core, axis=1, keepdims=False)
    theirs = lax.dynamic_index_in_dim(by_core, (core + 1) % cores, axis=1, keepdims=False)
    pairs = [(c, (c + 1) % cores) for c in range(cores)]
    chip_share = mine + lax.ppermute(theirs, "core", pairs)
    return lax.all_to_all(chip_share, CHIPS, split_axis=0, concat_axis=0, tiled=True)


def screen_kernel(live_ref, amp_ref, out_ref):
    n_a, _, rows = out_ref.shape
    nc = amp_ref.shape[2] // n_a
    for k in range(amp_ref.shape[1]):
        flipped = (amp_ref[:, k, :] * live_ref[:, k:k + 1]).T
        out_ref[:, k * nc:(k + 1) * nc, :] = flipped.reshape(n_a, nc, rows)


def screened_by_a(amplitudes, live, virtuals):
    rows, kblock, width = amplitudes.shape
    lanes = 128
    per_step = lanes // virtuals
    return pl.pallas_call(
        screen_kernel,
        grid=(width // lanes,),
        out_shape=jax.ShapeDtypeStruct((width // virtuals, kblock * virtuals, rows), jnp.float32),
        in_specs=[
            pl.BlockSpec((rows, kblock), lambda s: (0, 0)),
            pl.BlockSpec((rows, kblock, lanes), lambda s: (0, 0, s)),
        ],
        out_specs=pl.BlockSpec((per_step, kblock * virtuals, rows), lambda s: (s, 0, 0)),
    )(live, amplitudes)


def gathered_integrals(ladder_integrals):
    cores = lax.axis_size("core")
    core = lax.axis_index("core")
    chips = lax.axis_size(CHIPS)
    chip = lax.axis_index(CHIPS)
    sibling = lax.ppermute(ladder_integrals, "core", [(c, (c + 1) % cores) for c in range(cores)])
    pair = jnp.where(core == 0, jnp.concatenate([ladder_integrals, sibling], 0), jnp.concatenate([sibling, ladder_integrals], 0))
    half = pair.shape[1] // cores
    mine = lax.dynamic_slice_in_dim(pair, core * half, half, axis=1)
    blocks = [mine]
    for shift in range(1, chips):
        blocks.append(lax.ppermute(mine, CHIPS, [(q, (q + shift) % chips) for q in range(chips)]))
    by_shift = jnp.stack(blocks, 0)
    by_chip = jnp.take(by_shift, (chip - jnp.arange(chips)) % chips, axis=0)
    column = by_chip.reshape(-1, half)
    other = lax.ppermute(column, "core", [(c, (c + 1) % cores) for c in range(cores)])
    return jnp.where(core == 0, jnp.concatenate([column, other], 1), jnp.concatenate([other, column], 1))


def local(amplitudes, pair_live, ladder_integrals, cycle_integrals):
    live = pair_live.astype(jnp.float32)
    screened = amplitudes * live[:, :, None]
    first_rows = screened.shape[0]
    second_rows = screened.shape[1]
    width = screened.shape[2]
    virtuals = cycle_integrals.shape[1]

    weights = cycle_piece(cycle_integrals, second_rows)
    split = screened_by_a(amplitudes, live, virtuals).reshape(width // virtuals, second_rows, virtuals, first_rows)
    partial_value = jnp.einsum(
        "akci,kcm->aim",
        split,
        weights,
        precision=lax.Precision.HIGH,
        preferred_element_type=jnp.float32,
    )
    cycle_part = cycle_reduce(partial_value)

    flat = screened.reshape(first_rows * second_rows, width)
    ladder = jnp.dot(
        flat,
        gathered_integrals(ladder_integrals),
        precision=lax.Precision.HIGH,
        preferred_element_type=jnp.float32,
    )
    ladder_part = ladder.reshape(first_rows, second_rows, width) * live[:, :, None]
    ladder_part, cycle_part = lax.optimization_barrier((ladder_part, cycle_part))
    return (ladder_part, jnp.sum(cycle_part, axis=0)[:, None, :])


def solution(mesh):
    sizes = (4, 4, 2)
    named = Mesh(mesh.devices.reshape(sizes + (mesh.shape["vir"],)), PARTS + ("vir",))
    assert mesh.axis_names == ("own", "vir") and mesh.shape["own"] == 32
    placed = (P("vir", PARTS, None), P("vir", PARTS), P(PARTS, None), P("vir", None, None))
    return jax.shard_map(
        local,
        mesh=named,
        in_specs=placed,
        out_specs=(P("vir", PARTS, None), P("vir", PARTS, None)),
        check_vma=False,
    )
```

```python
import jax
import jax.numpy as jnp
from jax import lax
from jax.experimental import pallas as pl
from jax.experimental.pallas import tpu as pltpu
from jax.sharding import Mesh
from jax.sharding import PartitionSpec as P

PARTS = ("y", "z", "core")
CHIPS = ("y", "z")


def cycle_piece(cycle_integrals, kblock):
    own = lax.axis_index(PARTS)
    vir = lax.axis_index("vir")
    n_own = lax.axis_size(PARTS)
    n_vir = lax.axis_size("vir")
    held = cycle_integrals.shape[0]
    start = own * kblock
    piece = lax.dynamic_slice_in_dim(cycle_integrals, start % held, kblock, axis=0)
    holder = start // held
    chosen = piece
    for shift in range(1, n_vir):
        pairs = []
        for o in range(n_own):
            src = (o * kblock) // held
            dst = (src + shift) % n_vir
            pairs.append((o * n_vir + src, o * n_vir + dst))
        got = lax.ppermute(piece, PARTS + ("vir",), pairs)
        chosen = jnp.where((vir - holder) % n_vir == shift, got, chosen)
    return chosen


def cycle_reduce(partial_value):
    cores = lax.axis_size("core")
    core = lax.axis_index("core")
    rest = partial_value.shape[1:]
    by_core = partial_value.reshape((-1, cores) + rest)
    mine = lax.dynamic_index_in_dim(by_core, core, axis=1, keepdims=False)
    theirs = lax.dynamic_index_in_dim(by_core, (core + 1) % cores, axis=1, keepdims=False)
    pairs = [(c, (c + 1) % cores) for c in range(cores)]
    chip_share = mine + lax.ppermute(theirs, "core", pairs)
    return lax.all_to_all(chip_share, CHIPS, split_axis=0, concat_axis=0, tiled=True)


def screen_kernel(live_ref, amp_ref, out_ref):
    n_a, _, rows = out_ref.shape
    nc = amp_ref.shape[2] // n_a
    for k in range(amp_ref.shape[1]):
        flipped = (amp_ref[:, k, :] * live_ref[:, k:k + 1]).T
        out_ref[:, k * nc:(k + 1) * nc, :] = flipped.reshape(n_a, nc, rows)


def screened_by_a(amplitudes, live, virtuals):
    rows, kblock, width = amplitudes.shape
    lanes = 128
    per_step = lanes // virtuals
    return pl.pallas_call(
        screen_kernel,
        grid=(width // lanes,),
        out_shape=jax.ShapeDtypeStruct((width // virtuals, kblock * virtuals, rows), jnp.float32),
        in_specs=[
            pl.BlockSpec((rows, kblock), lambda s: (0, 0)),
            pl.BlockSpec((rows, kblock, lanes), lambda s: (0, 0, s)),
        ],
        out_specs=pl.BlockSpec((per_step, kblock * virtuals, rows), lambda s: (s, 0, 0)),
    )(live, amplitudes)


def local(amplitudes, pair_live, ladder_integrals, cycle_integrals):
    live = pair_live.astype(jnp.float32)
    screened = amplitudes * live[:, :, None]
    first_rows = screened.shape[0]
    second_rows = screened.shape[1]
    width = screened.shape[2]
    virtuals = cycle_integrals.shape[1]

    weights = cycle_piece(cycle_integrals, second_rows)
    split = screened_by_a(amplitudes, live, virtuals).reshape(width // virtuals, second_rows, virtuals, first_rows)
    partial_value = jnp.einsum(
        "akci,kcm->aim",
        split,
        weights,
        precision=lax.Precision.HIGH,
        preferred_element_type=jnp.float32,
    )
    cycle_part = cycle_reduce(partial_value)

    flat = amplitudes.reshape(first_rows * second_rows, width)
    ladder = jnp.dot(
        flat,
        lax.all_gather(ladder_integrals, PARTS, axis=0, tiled=True),
        precision=lax.Precision.HIGH,
        preferred_element_type=jnp.float32,
    )
    ladder_part = ladder.reshape(first_rows, second_rows, width) * live[:, :, None]
    ladder_part, cycle_part = lax.optimization_barrier((ladder_part, cycle_part))
    return (ladder_part, jnp.sum(cycle_part, axis=0)[:, None, :])


def solution(mesh):
    sizes = (4, 4, 2)
    named = Mesh(mesh.devices.reshape(sizes + (mesh.shape["vir"],)), PARTS + ("vir",))
    assert mesh.axis_names == ("own", "vir") and mesh.shape["own"] == 32
    placed = (P("vir", PARTS, None), P("vir", PARTS), P(PARTS, None), P("vir", None, None))
    return jax.shard_map(
        local,
        mesh=named,
        in_specs=placed,
        out_specs=(P("vir", PARTS, None), P("vir", PARTS, None)),
        check_vma=False,
    )
```

```python
import jax
import jax.numpy as jnp
from jax import lax
from jax.experimental import pallas as pl
from jax.experimental.pallas import tpu as pltpu
from jax.sharding import Mesh
from jax.sharding import PartitionSpec as P

PARTS = ("y", "z", "core")
CHIPS = ("y", "z")


def cycle_piece(cycle_integrals, kblock):
    own = lax.axis_index(PARTS)
    vir = lax.axis_index("vir")
    n_own = lax.axis_size(PARTS)
    n_vir = lax.axis_size("vir")
    held = cycle_integrals.shape[0]
    start = own * kblock
    piece = lax.dynamic_slice_in_dim(cycle_integrals, start % held, kblock, axis=0)
    holder = start // held
    chosen = piece
    for shift in range(1, n_vir):
        pairs = []
        for o in range(n_own):
            src = (o * kblock) // held
            dst = (src + shift) % n_vir
            pairs.append((o * n_vir + src, o * n_vir + dst))
        got = lax.ppermute(piece, PARTS + ("vir",), pairs)
        chosen = jnp.where((vir - holder) % n_vir == shift, got, chosen)
    return chosen


def cycle_reduce(partial_value):
    cores = lax.axis_size("core")
    core = lax.axis_index("core")
    rest = partial_value.shape[1:]
    by_core = partial_value.reshape((-1, cores) + rest)
    mine = lax.dynamic_index_in_dim(by_core, core, axis=1, keepdims=False)
    theirs = lax.dynamic_index_in_dim(by_core, (core + 1) % cores, axis=1, keepdims=False)
    pairs = [(c, (c + 1) % cores) for c in range(cores)]
    chip_share = mine + lax.ppermute(theirs, "core", pairs)
    return chip_share


def screen_kernel(live_ref, amp_ref, out_ref):
    n_a, _, rows = out_ref.shape
    nc = amp_ref.shape[2] // n_a
    for k in range(amp_ref.shape[1]):
        flipped = (amp_ref[:, k, :] * live_ref[:, k:k + 1]).T
        out_ref[:, k * nc:(k + 1) * nc, :] = flipped.reshape(n_a, nc, rows)


def screened_by_a(amplitudes, live, virtuals):
    rows, kblock, width = amplitudes.shape
    lanes = 128
    per_step = lanes // virtuals
    return pl.pallas_call(
        screen_kernel,
        grid=(width // lanes,),
        out_shape=jax.ShapeDtypeStruct((width // virtuals, kblock * virtuals, rows), jnp.float32),
        in_specs=[
            pl.BlockSpec((rows, kblock), lambda s: (0, 0)),
            pl.BlockSpec((rows, kblock, lanes), lambda s: (0, 0, s)),
        ],
        out_specs=pl.BlockSpec((per_step, kblock * virtuals, rows), lambda s: (s, 0, 0)),
    )(live, amplitudes)


def local(amplitudes, pair_live, ladder_integrals, cycle_integrals):
    live = pair_live.astype(jnp.float32)
    screened = amplitudes * live[:, :, None]
    first_rows = screened.shape[0]
    second_rows = screened.shape[1]
    width = screened.shape[2]
    virtuals = cycle_integrals.shape[1]

    weights = cycle_piece(cycle_integrals, second_rows)
    split = screened_by_a(amplitudes, live, virtuals).reshape(width // virtuals, second_rows, virtuals, first_rows)
    partial_value = jnp.einsum(
        "akci,kcm->aim",
        split,
        weights,
        precision=lax.Precision.HIGH,
        preferred_element_type=jnp.float32,
    )
    cycle_part = cycle_reduce(partial_value)

    flat = amplitudes.reshape(first_rows * second_rows, width)
    full = lax.all_gather(ladder_integrals, PARTS, axis=0, tiled=True)
    cycle_part, _ = lax.optimization_barrier((cycle_part, full))
    cycle_part = lax.all_to_all(cycle_part, CHIPS, split_axis=0, concat_axis=0, tiled=True)
    ladder = jnp.dot(
        flat,
        full,
        precision=lax.Precision.HIGH,
        preferred_element_type=jnp.float32,
    )
    ladder_part = ladder.reshape(first_rows, second_rows, width) * live[:, :, None]
    ladder_part, cycle_part = lax.optimization_barrier((ladder_part, cycle_part))
    return (ladder_part, jnp.sum(cycle_part, axis=0)[:, None, :])


def solution(mesh):
    sizes = (4, 4, 2)
    named = Mesh(mesh.devices.reshape(sizes + (mesh.shape["vir"],)), PARTS + ("vir",))
    assert mesh.axis_names == ("own", "vir") and mesh.shape["own"] == 32
    placed = (P("vir", PARTS, None), P("vir", PARTS), P(PARTS, None), P("vir", None, None))
    return jax.shard_map(
        local,
        mesh=named,
        in_specs=placed,
        out_specs=(P("vir", PARTS, None), P("vir", PARTS, None)),
        check_vma=False,
    )
```

```python
import jax
import jax.numpy as jnp
from jax import lax
from jax.experimental import pallas as pl
from jax.experimental.pallas import tpu as pltpu
from jax.sharding import Mesh
from jax.sharding import PartitionSpec as P

PARTS = ("y", "z", "core")
CHIPS = ("y", "z")


def cycle_piece(cycle_integrals, kblock):
    own = lax.axis_index(PARTS)
    vir = lax.axis_index("vir")
    n_own = lax.axis_size(PARTS)
    n_vir = lax.axis_size("vir")
    held = cycle_integrals.shape[0]
    start = own * kblock
    piece = lax.dynamic_slice_in_dim(cycle_integrals, start % held, kblock, axis=0)
    holder = start // held
    chosen = piece
    for shift in range(1, n_vir):
        pairs = []
        for o in range(n_own):
            src = (o * kblock) // held
            dst = (src + shift) % n_vir
            pairs.append((o * n_vir + src, o * n_vir + dst))
        got = lax.ppermute(piece, PARTS + ("vir",), pairs)
        chosen = jnp.where((vir - holder) % n_vir == shift, got, chosen)
    return chosen


def cycle_reduce(partial_value):
    cores = lax.axis_size("core")
    core = lax.axis_index("core")
    rest = partial_value.shape[1:]
    by_core = partial_value.reshape((-1, cores) + rest)
    mine = lax.dynamic_index_in_dim(by_core, core, axis=1, keepdims=False)
    theirs = lax.dynamic_index_in_dim(by_core, (core + 1) % cores, axis=1, keepdims=False)
    pairs = [(c, (c + 1) % cores) for c in range(cores)]
    chip_share = mine + lax.ppermute(theirs, "core", pairs)
    return lax.all_to_all(chip_share, CHIPS, split_axis=0, concat_axis=0, tiled=True)


def screen_kernel(live_ref, amp_ref, out_ref):
    n_a, _, rows = out_ref.shape
    nc = amp_ref.shape[2] // n_a
    for k in range(amp_ref.shape[1]):
        flipped = (amp_ref[:, k, :] * live_ref[:, k:k + 1]).T
        out_ref[:, k * nc:(k + 1) * nc, :] = flipped.reshape(n_a, nc, rows)


def screened_by_a(amplitudes, live, virtuals):
    rows, kblock, width = amplitudes.shape
    lanes = 128
    per_step = lanes // virtuals
    return pl.pallas_call(
        screen_kernel,
        grid=(width // lanes,),
        out_shape=jax.ShapeDtypeStruct((width // virtuals, kblock * virtuals, rows), jnp.float32),
        in_specs=[
            pl.BlockSpec((rows, kblock), lambda s: (0, 0)),
            pl.BlockSpec((rows, kblock, lanes), lambda s: (0, 0, s)),
        ],
        out_specs=pl.BlockSpec((per_step, kblock * virtuals, rows), lambda s: (s, 0, 0)),
    )(live, amplitudes)


def local(amplitudes, pair_live, ladder_integrals, cycle_integrals):
    live = pair_live.astype(jnp.float32)
    screened = amplitudes * live[:, :, None]
    first_rows = screened.shape[0]
    second_rows = screened.shape[1]
    width = screened.shape[2]
    virtuals = cycle_integrals.shape[1]

    weights = cycle_piece(cycle_integrals, second_rows)
    split = screened_by_a(amplitudes, live, virtuals).reshape(width // virtuals, second_rows, virtuals, first_rows)
    partial_value = jnp.einsum(
        "akci,kcm->aim",
        split,
        weights,
        precision=lax.Precision.HIGHEST,
        preferred_element_type=jnp.float32,
    )
    cycle_part = cycle_reduce(partial_value)

    flat = amplitudes.reshape(first_rows * second_rows, width)
    ladder = jnp.dot(
        flat,
        lax.all_gather(ladder_integrals, PARTS, axis=0, tiled=True),
        precision=lax.Precision.HIGH,
        preferred_element_type=jnp.float32,
    )
    ladder_part = ladder.reshape(first_rows, second_rows, width) * live[:, :, None]
    ladder_part, cycle_part = lax.optimization_barrier((ladder_part, cycle_part))
    return (ladder_part, jnp.sum(cycle_part, axis=0)[:, None, :])


def solution(mesh):
    sizes = (4, 4, 2)
    named = Mesh(mesh.devices.reshape(sizes + (mesh.shape["vir"],)), PARTS + ("vir",))
    assert mesh.axis_names == ("own", "vir") and mesh.shape["own"] == 32
    placed = (P("vir", PARTS, None), P("vir", PARTS), P(PARTS, None), P("vir", None, None))
    return jax.shard_map(
        local,
        mesh=named,
        in_specs=placed,
        out_specs=(P("vir", PARTS, None), P("vir", PARTS, None)),
        check_vma=False,
    )
```

```python
import jax
import jax.numpy as jnp
from jax import lax
from jax.experimental import pallas as pl
from jax.experimental.pallas import tpu as pltpu
from jax.sharding import Mesh
from jax.sharding import PartitionSpec as P

PARTS = ("y", "z", "core")
CHIPS = ("y", "z")


def cycle_piece(cycle_integrals, kblock):
    own = lax.axis_index(PARTS)
    vir = lax.axis_index("vir")
    n_own = lax.axis_size(PARTS)
    n_vir = lax.axis_size("vir")
    held = cycle_integrals.shape[0]
    start = own * kblock
    piece = lax.dynamic_slice_in_dim(cycle_integrals, start % held, kblock, axis=0)
    holder = start // held
    chosen = piece
    for shift in range(1, n_vir):
        pairs = []
        for o in range(n_own):
            src = (o * kblock) // held
            dst = (src + shift) % n_vir
            pairs.append((o * n_vir + src, o * n_vir + dst))
        got = lax.ppermute(piece, PARTS + ("vir",), pairs)
        chosen = jnp.where((vir - holder) % n_vir == shift, got, chosen)
    return chosen


def cycle_reduce(partial_value):
    cores = lax.axis_size("core")
    core = lax.axis_index("core")
    rest = partial_value.shape[1:]
    by_core = partial_value.reshape((-1, cores) + rest)
    mine = lax.dynamic_index_in_dim(by_core, core, axis=1, keepdims=False)
    theirs = lax.dynamic_index_in_dim(by_core, (core + 1) % cores, axis=1, keepdims=False)
    pairs = [(c, (c + 1) % cores) for c in range(cores)]
    chip_share = mine + lax.ppermute(theirs, "core", pairs)
    return lax.all_to_all(chip_share, CHIPS, split_axis=0, concat_axis=0, tiled=True)


def screen_kernel(live_ref, amp_ref, out_ref):
    n_a, _, rows = out_ref.shape
    nc = amp_ref.shape[2] // n_a
    for k in range(amp_ref.shape[1]):
        flipped = (amp_ref[:, k, :] * live_ref[:, k:k + 1]).T
        out_ref[:, k * nc:(k + 1) * nc, :] = flipped.reshape(n_a, nc, rows)


def screened_by_a(amplitudes, live, virtuals):
    rows, kblock, width = amplitudes.shape
    lanes = 128
    per_step = lanes // virtuals
    return pl.pallas_call(
        screen_kernel,
        grid=(width // lanes,),
        out_shape=jax.ShapeDtypeStruct((width // virtuals, kblock * virtuals, rows), jnp.float32),
        in_specs=[
            pl.BlockSpec((rows, kblock), lambda s: (0, 0)),
            pl.BlockSpec((rows, kblock, lanes), lambda s: (0, 0, s)),
        ],
        out_specs=pl.BlockSpec((per_step, kblock * virtuals, rows), lambda s: (s, 0, 0)),
    )(live, amplitudes)


def local(amplitudes, pair_live, ladder_integrals, cycle_integrals):
    live = pair_live.astype(jnp.float32)
    screened = amplitudes * live[:, :, None]
    first_rows = screened.shape[0]
    second_rows = screened.shape[1]
    width = screened.shape[2]
    virtuals = cycle_integrals.shape[1]

    by_a = screened_by_a(amplitudes, live, virtuals)
    held, by_a = lax.optimization_barrier((cycle_integrals, by_a))
    weights = cycle_piece(held, second_rows)
    split = by_a.reshape(width // virtuals, second_rows, virtuals, first_rows)
    partial_value = jnp.einsum(
        "akci,kcm->aim",
        split,
        weights,
        precision=lax.Precision.HIGHEST,
        preferred_element_type=jnp.float32,
    )
    cycle_part = cycle_reduce(partial_value)

    flat = amplitudes.reshape(first_rows * second_rows, width)
    ladder = jnp.dot(
        flat,
        lax.all_gather(ladder_integrals, PARTS, axis=0, tiled=True),
        precision=lax.Precision.HIGH,
        preferred_element_type=jnp.float32,
    )
    ladder_part = ladder.reshape(first_rows, second_rows, width) * live[:, :, None]
    ladder_part, cycle_part = lax.optimization_barrier((ladder_part, cycle_part))
    return (ladder_part, jnp.sum(cycle_part, axis=0)[:, None, :])


def solution(mesh):
    sizes = (4, 4, 2)
    named = Mesh(mesh.devices.reshape(sizes + (mesh.shape["vir"],)), PARTS + ("vir",))
    assert mesh.axis_names == ("own", "vir") and mesh.shape["own"] == 32
    placed = (P("vir", PARTS, None), P("vir", PARTS), P(PARTS, None), P("vir", None, None))
    return jax.shard_map(
        local,
        mesh=named,
        in_specs=placed,
        out_specs=(P("vir", PARTS, None), P("vir", PARTS, None)),
        check_vma=False,
    )
```

```python
import jax
import jax.numpy as jnp
from jax import lax
from jax.experimental import pallas as pl
from jax.experimental.pallas import tpu as pltpu
from jax.sharding import Mesh
from jax.sharding import PartitionSpec as P

PARTS = ("y", "z", "core")
CHIPS = ("y", "z")


def cycle_piece(cycle_integrals, kblock):
    own = lax.axis_index(PARTS)
    vir = lax.axis_index("vir")
    n_own = lax.axis_size(PARTS)
    n_vir = lax.axis_size("vir")
    held = cycle_integrals.shape[0]
    start = own * kblock
    piece = lax.dynamic_slice_in_dim(cycle_integrals, start % held, kblock, axis=0)
    holder = start // held
    chosen = piece
    for shift in range(1, n_vir):
        pairs = []
        for o in range(n_own):
            src = (o * kblock) // held
            dst = (src + shift) % n_vir
            pairs.append((o * n_vir + src, o * n_vir + dst))
        got = lax.ppermute(piece, PARTS + ("vir",), pairs)
        chosen = jnp.where((vir - holder) % n_vir == shift, got, chosen)
    return chosen


def cycle_reduce(partial_value):
    cores = lax.axis_size("core")
    core = lax.axis_index("core")
    rest = partial_value.shape[1:]
    by_core = partial_value.reshape((-1, cores) + rest)
    mine = lax.dynamic_index_in_dim(by_core, core, axis=1, keepdims=False)
    theirs = lax.dynamic_index_in_dim(by_core, (core + 1) % cores, axis=1, keepdims=False)
    pairs = [(c, (c + 1) % cores) for c in range(cores)]
    chip_share = mine + lax.ppermute(theirs, "core", pairs)
    return lax.all_to_all(chip_share, CHIPS, split_axis=0, concat_axis=0, tiled=True)


def screen_kernel(live_ref, amp_ref, out_ref):
    n_a, _, rows = out_ref.shape
    nc = amp_ref.shape[2] // n_a
    for k in range(amp_ref.shape[1]):
        flipped = (amp_ref[:, k, :] * live_ref[:, k:k + 1]).T
        out_ref[:, k * nc:(k + 1) * nc, :] = flipped.reshape(n_a, nc, rows)


def screened_by_a(amplitudes, live, virtuals):
    rows, kblock, width = amplitudes.shape
    lanes = 256
    per_step = lanes // virtuals
    return pl.pallas_call(
        screen_kernel,
        grid=(width // lanes,),
        out_shape=jax.ShapeDtypeStruct((width // virtuals, kblock * virtuals, rows), jnp.float32),
        in_specs=[
            pl.BlockSpec((rows, kblock), lambda s: (0, 0)),
            pl.BlockSpec((rows, kblock, lanes), lambda s: (0, 0, s)),
        ],
        out_specs=pl.BlockSpec((per_step, kblock * virtuals, rows), lambda s: (s, 0, 0)),
    )(live, amplitudes)


def local(amplitudes, pair_live, ladder_integrals, cycle_integrals):
    live = pair_live.astype(jnp.float32)
    screened = amplitudes * live[:, :, None]
    first_rows = screened.shape[0]
    second_rows = screened.shape[1]
    width = screened.shape[2]
    virtuals = cycle_integrals.shape[1]

    weights = cycle_piece(cycle_integrals, second_rows)
    split = screened_by_a(amplitudes, live, virtuals).reshape(width // virtuals, second_rows, virtuals, first_rows)
    partial_value = jnp.einsum(
        "akci,kcm->aim",
        split,
        weights,
        precision=lax.Precision.HIGHEST,
        preferred_element_type=jnp.float32,
    )
    cycle_part = cycle_reduce(partial_value)

    flat = amplitudes.reshape(first_rows * second_rows, width)
    ladder = jnp.dot(
        flat,
        lax.all_gather(ladder_integrals, PARTS, axis=0, tiled=True),
        precision=lax.Precision.HIGH,
        preferred_element_type=jnp.float32,
    )
    ladder_part = ladder.reshape(first_rows, second_rows, width) * live[:, :, None]
    ladder_part, cycle_part = lax.optimization_barrier((ladder_part, cycle_part))
    return (ladder_part, jnp.sum(cycle_part, axis=0)[:, None, :])


def solution(mesh):
    sizes = (4, 4, 2)
    named = Mesh(mesh.devices.reshape(sizes + (mesh.shape["vir"],)), PARTS + ("vir",))
    assert mesh.axis_names == ("own", "vir") and mesh.shape["own"] == 32
    placed = (P("vir", PARTS, None), P("vir", PARTS), P(PARTS, None), P("vir", None, None))
    return jax.shard_map(
        local,
        mesh=named,
        in_specs=placed,
        out_specs=(P("vir", PARTS, None), P("vir", PARTS, None)),
        check_vma=False,
    )
```
